256 devices in a mesh: section: 4 (over x_lo, core), dp: 8 (over y, x_hi), expert: 8 (over z).
Axes of the slice: x: 4 (x_hi: 2, x_lo: 2; x = x_hi * 2 + x_lo), y: 4, z: 8, core: 2. Of those that a mesh axis runs over, the one named last changes fastest.
Arguments:
- incoming: bfloat16 [4, 2, 1024, 3584], P('section', None, ('dp', 'expert')), may hold values from -6 to 6
- stash: bfloat16 [4, 2, 1024, 3584], P('section', None, ('dp', 'expert')), may hold values from -6 to 6
- expert_ids: int32 [4, 2, 1024, 2], P('section', None, ('dp', 'expert')), may hold values from 0 to 7, all different within a row; in each aligned block of 16 rows (0 to 15, 16 to 31, ..., all dimensions but the last counted through in order) at most 6 rows name the same one
- route_weight: float32 [4, 2, 1024, 2], P('section', None, ('dp', 'expert')), may hold values from 0.1 to 1
- w_gate: bfloat16 [4, 8, 3584, 2048], P('section', 'expert', None, 'dp'), may hold values from -0.09375 to 0.09375
- w_up: bfloat16 [4, 8, 3584, 2048], P('section', 'expert', None, 'dp'), may hold values from -0.09375 to 0.09375
- w_down: bfloat16 [4, 8, 2048, 3584], P('section', 'expert', 'dp'), may hold values from -0.125 to 0.125
Outputs:
- input_grad: bfloat16 [4, 2, 1024, 3584], P('section', None, ('dp', 'expert'))
- grad_gate: bfloat16 [4, 8, 3584, 2048], P('section', 'expert', None, 'dp')
- grad_up: bfloat16 [4, 8, 3584, 2048], P('section', 'expert', None, 'dp')
- grad_down: bfloat16 [4, 8, 2048, 3584], P('section', 'expert', 'dp')
The draws below stay inside these ranges and needn't reach their ends.
Inputs may be any that keep to these rules, and one draw needn't show every extreme that they name: `expert_ids`: each token names 2 different experts. Among the 16 tokens of one device in one micro-batch (aligned blocks of rows), no expert is named by more than 6 of them, a bound that some block reaches.
All inputs are finite; a program needn't handle non-finite values.
Results may differ from the reference program's by a relative error of at most 0.01.
Values may be sent and summed in bfloat16 or wider, within the bound.
No kernel may reach another device: no remote copies, remote signals or barrier semaphores. Data moves between devices by JAX's collectives and lax.ppermute only.
A program may use at most 128 MiB of HBM per device.

```python
import math
import jax
import jax.numpy as jnp
import numpy as np
from jax import lax

D = 3584
HID = 2048
TOPK = 2
MB = 2
TOK_DEV = 16
EXPERTS = 8
CAP = 6
TOKENS = 1024
N_SECTION = 4
N_DP = 8


def block_scale(own_key, dims, split, low, top_value):
    def one(dim, parts):
        heights = jax.random.uniform(jax.random.fold_in(jax.random.fold_in(own_key, 6), dim), (parts,), jnp.float32, low / len(split), top_value / len(split))
        return jnp.repeat(jnp.exp(heights), dims[dim] // parts).reshape((-1,) + (1,) * (len(dims) - dim - 1))

    loudness = one(*split[0])
    for cut in split[1:]:
        loudness = loudness * one(*cut)
    return loudness


def deal_out(key, own, number, rows, amount, top, limit, skew):
    order = jax.random.permutation(key, amount)
    crowded, common = shares(amount, rows * top, limit, skew, True), shares(amount, rows * top, limit, skew, False)
    places = jnp.arange(amount)

    def named(sizes, offset_by):
        used = int((sizes > 0).sum())
        fixed = max(1, used // 4)
        moved = fixed + (places - fixed + offset_by * (used - fixed)) % max(1, amount - fixed)
        return jnp.zeros((amount,), jnp.int32).at[order[jnp.where(places < fixed, places, moved)]].set(jnp.asarray(sizes, jnp.int32))

    sizes = jnp.where(number % 4 == 0, named(crowded, number // 4), named(common, number - number // 4 - 1))
    mixed = jax.random.permutation(jax.random.fold_in(own, 3), amount)
    donor, taker = mixed[0:amount // 2 * 2:2], mixed[1:amount // 2 * 2:2]
    room = jnp.minimum(sizes[donor] - 1, limit - sizes[taker]) // 2
    room = jnp.where((donor == order[0]) | (taker == order[0]) | (sizes[taker] == 0), 0, jnp.maximum(room, 0))
    moved = jax.random.randint(jax.random.fold_in(own, 4), (amount // 2,), 0, 1 << 20) % (room + 1)
    sizes = sizes.at[donor].add(-moved).at[taker].add(moved)
    items = jnp.searchsorted(jnp.cumsum(sizes), jnp.arange(rows * top), side="right").astype(jnp.int32)
    table = items.reshape(top, rows).T
    table = table[jax.random.permutation(jax.random.fold_in(own, 1), rows)]
    offset_by = jax.random.randint(jax.random.fold_in(own, 2), (rows, 1), 0, top)
    return jnp.take_along_axis(table, (jnp.arange(top)[None, :] + offset_by) % top, axis=1)


def shares(count, total, reach, skew, full):
    weights = [(1 << 20) // math.isqrt(rank ** skew) + 1 for rank in range(1, count + 1)]
    largest = reach if full else min(reach, max(-(-total // count), total * weights[0] // sum(weights)))
    least = 1 if total - largest >= count - 1 else 0
    given, surplus = [largest] + [least] * (count - 1), total - largest - least * (count - 1)
    while surplus > 0:
        movable = [i for i in range(1, count) if given[i] < largest] or [i for i in range(1, count) if given[i] < reach]
        pool, budget = sum([weights[i] for i in movable]), surplus
        for i in movable:
            extra = min(reach - given[i], max(1, budget * weights[i] // pool), surplus)
            given[i] = given[i] + extra
            surplus = surplus - extra
    return np.array(given)


def bell_draw(rng, extent, spread, limit, pieces=(), kind=jnp.bfloat16):
    loudness = block_scale(rng, extent, pieces, -0.22, 0.18) if pieces else 1.0
    result = jax.random.normal(rng, extent, jnp.float32) * spread * loudness
    return jnp.minimum(jnp.maximum(result, -limit), limit).astype(kind)


def setup_inputs(seed: int = 0) -> dict:
    streams_of = jax.random.split(jax.random.key(seed), 8)
    incoming = bell_draw(streams_of[0], (N_SECTION, MB, TOKENS, D), 1.0, 6.0, ((0, 4), (2, 64)))
    stash = bell_draw(streams_of[1], (N_SECTION, MB, TOKENS, D), 1.0, 6.0, ((0, 4), (2, 64)))
    expert_ids_keys = jax.random.split(jax.random.fold_in(streams_of[2], 1), N_SECTION * MB * TOKENS // TOK_DEV)
    expert_ids_turns = jax.random.permutation(jax.random.fold_in(streams_of[2], 3), N_SECTION * MB * TOKENS // TOK_DEV)
    expert_ids = jax.vmap(lambda own, number: deal_out(jax.random.fold_in(streams_of[2], 2), own, number, TOK_DEV, EXPERTS, TOPK, CAP, 2))(expert_ids_keys, expert_ids_turns).reshape((N_SECTION, MB, TOKENS, TOPK))
    route_weight = jnp.clip(0.1 + 0.9 * jax.random.uniform(streams_of[3], (N_SECTION, MB, TOKENS, TOPK), jnp.float32) ** block_scale(streams_of[3], (N_SECTION, MB, TOKENS, TOPK), ((0, 4), (2, 64)), -0.2, 0.2), 0.1, 1.0)
    w_gate = bell_draw(streams_of[4], (N_SECTION, EXPERTS, D, HID), D ** -0.5, 0.09375, ((0, 4), (1, 8), (3, 8)))
    w_up = bell_draw(streams_of[5], (N_SECTION, EXPERTS, D, HID), D ** -0.5, 0.09375, ((0, 4), (1, 8), (3, 8)))
    w_down = bell_draw(streams_of[6], (N_SECTION, EXPERTS, HID, D), HID ** -0.5, 0.125, ((0, 4), (1, 8), (2, 8)))
    return dict(incoming=incoming, stash=stash, expert_ids=expert_ids, route_weight=route_weight, w_gate=w_gate, w_up=w_up, w_down=w_down)


def reference(incoming, stash, expert_ids, route_weight, w_gate, w_up, w_down):
    upstream_all = jnp.roll(incoming, -1, axis=0)
    groups = N_DP * EXPERTS
    pair_count = TOK_DEV * TOPK
    block_width = HID // N_DP
    row_total = MB * groups * CAP
    batch_index = jnp.arange(MB, dtype=jnp.int32)[:, None, None]
    group_index = jnp.arange(groups, dtype=jnp.int32)[None, :, None]
    input_grads = []
    gate_sections = []
    up_sections = []
    down_sections = []
    for section_index in range(N_SECTION):
        upstream = upstream_all[section_index].reshape(MB, groups, TOK_DEV, D)
        tokens = stash[section_index].reshape(MB, groups, TOK_DEV, D)
        chosen = expert_ids[section_index].reshape(MB, groups, pair_count).astype(jnp.int32)
        weight_pairs = route_weight[section_index].reshape(MB, groups, pair_count)
        onehot = (chosen[..., None] == jnp.arange(EXPERTS, dtype=jnp.int32)).astype(jnp.int32)
        running = jnp.cumsum(onehot, axis=2).astype(jnp.int32) - 1
        position = jnp.sum(onehot * running, axis=3).astype(jnp.int32)
        slot_index = (chosen * CAP + position).astype(jnp.int32)
        pair_inputs = jnp.repeat(tokens, TOPK, axis=2)
        pair_scaled = (weight_pairs[..., None] * jnp.repeat(upstream, TOPK, axis=2).astype(jnp.float32)).astype(jnp.bfloat16)
        empty_slots = jnp.zeros((MB, groups, EXPERTS * CAP, D), jnp.bfloat16)
        input_slots = empty_slots.at[batch_index, group_index, slot_index].set(pair_inputs).reshape(MB, groups, EXPERTS, CAP, D)
        scaled_slots = empty_slots.at[batch_index, group_index, slot_index].set(pair_scaled).reshape(MB, groups, EXPERTS, CAP, D)
        backs = []
        gate_experts = []
        up_experts = []
        down_experts = []
        for expert_index in range(EXPERTS):
            input_rows = input_slots[:, :, expert_index].reshape(row_total, D)
            scaled_rows = scaled_slots[:, :, expert_index].reshape(row_total, D)
            gate_full = w_gate[section_index, expert_index]
            up_full = w_up[section_index, expert_index]
            down_full = w_down[section_index, expert_index]
            gate_pre = jnp.dot(input_rows, gate_full, preferred_element_type=jnp.float32)
            up_pre = jnp.dot(input_rows, up_full, preferred_element_type=jnp.float32)
            logistic = jax.nn.sigmoid(gate_pre)
            activated = gate_pre * logistic
            hidden = (activated * up_pre).astype(jnp.bfloat16)
            hidden_grad = jnp.dot(scaled_rows, down_full.T, preferred_element_type=jnp.float32)
            gate_grad = (hidden_grad * up_pre * logistic * (1.0 + gate_pre * (1.0 - logistic))).astype(jnp.bfloat16)
            up_grad = (hidden_grad * activated).astype(jnp.bfloat16)
            down_experts.append(jnp.dot(hidden.T, scaled_rows, preferred_element_type=jnp.float32).astype(jnp.bfloat16))
            gate_experts.append(jnp.dot(input_rows.T, gate_grad, preferred_element_type=jnp.float32).astype(jnp.bfloat16))
            up_experts.append(jnp.dot(input_rows.T, up_grad, preferred_element_type=jnp.float32).astype(jnp.bfloat16))
            gate_blocks = gate_grad.astype(jnp.float32).reshape(row_total, N_DP, block_width)
            up_blocks = up_grad.astype(jnp.float32).reshape(row_total, N_DP, block_width)
            gate_weights = gate_full.astype(jnp.float32).reshape(D, N_DP, block_width)
            up_weights = up_full.astype(jnp.float32).reshape(D, N_DP, block_width)
            partial_value = jnp.einsum("rnh,dnh->rnd", gate_blocks, gate_weights) + jnp.einsum("rnh,dnh->rnd", up_blocks, up_weights)
            rounded = lax.optimization_barrier(partial_value.astype(jnp.bfloat16)).astype(jnp.float32)
            pair_back = lax.optimization_barrier(jnp.sum(rounded, axis=1).astype(jnp.bfloat16))
            backs.append(pair_back.reshape(MB, groups, CAP, D))
        back_slots = jnp.stack(backs, axis=2).reshape(MB, groups, EXPERTS * CAP, D)
        per_pair = back_slots[batch_index, group_index, slot_index].astype(jnp.float32).reshape(MB, groups, TOK_DEV, TOPK, D)
        section_grad = (upstream.astype(jnp.float32) + jnp.sum(per_pair, axis=3)).astype(jnp.bfloat16)
        input_grads.append(section_grad.reshape(MB, groups * TOK_DEV, D))
        gate_sections.append(jnp.stack(gate_experts))
        up_sections.append(jnp.stack(up_experts))
        down_sections.append(jnp.stack(down_experts))
    return (jnp.stack(input_grads), jnp.stack(gate_sections), jnp.stack(up_sections), jnp.stack(down_sections))
```

```python
import jax
import jax.numpy as jnp
from jax import lax
from jax.sharding import PartitionSpec as P


def passed_along(x, axis, by):
    length = lax.axis_size(axis)
    return lax.ppermute(x, axis, [(i, (i + by) % length) for i in range(length)])


def slice_backward(pair_inputs, pair_scaled, gate_slice, up_slice, down_slice):
    contract_rows = (((0,), (0,)), ((), ()))
    contract_last = (((1,), (1,)), ((), ()))
    gate_pre = jnp.dot(pair_inputs, gate_slice, preferred_element_type=jnp.float32)
    up_pre = jnp.dot(pair_inputs, up_slice, preferred_element_type=jnp.float32)
    logistic = jax.nn.sigmoid(gate_pre)
    activated = gate_pre * logistic
    hidden = (activated * up_pre).astype(jnp.bfloat16)
    hidden_grad = lax.dot_general(
        pair_scaled, down_slice, contract_last, preferred_element_type=jnp.float32
    )
    gate_grad = (hidden_grad * up_pre * logistic * (1.0 + gate_pre * (1.0 - logistic))).astype(
        jnp.bfloat16
    )
    up_grad = (hidden_grad * activated).astype(jnp.bfloat16)
    down_total = lax.dot_general(
        hidden, pair_scaled, contract_rows, preferred_element_type=jnp.float32
    )
    gate_total = lax.dot_general(
        pair_inputs, gate_grad, contract_rows, preferred_element_type=jnp.float32
    )
    up_total = lax.dot_general(
        pair_inputs, up_grad, contract_rows, preferred_element_type=jnp.float32
    )
    partial_back = lax.dot_general(
        gate_grad, gate_slice, contract_last, preferred_element_type=jnp.float32
    )
    partial_back = partial_back + lax.dot_general(
        up_grad, up_slice, contract_last, preferred_element_type=jnp.float32
    )
    return (partial_back, gate_total, up_total, down_total)


def per_device(incoming, stash, expert_ids, route_weight, w_gate, w_up, w_down):
    arrived = passed_along(incoming, "section", -1)
    upstream = arrived[0]
    tokens = stash[0]
    mbatch, tok_rows, model_width = tokens.shape
    top_count = expert_ids.shape[-1]
    experts = lax.axis_size("expert")
    capacity = max(2, 3 * tok_rows * top_count // (2 * experts))
    pair_count = tok_rows * top_count
    slot_count = experts * capacity
    chosen = expert_ids[0].reshape(mbatch, pair_count)
    onehot = (chosen[:, :, None] == jnp.arange(experts, dtype=jnp.int32)[None, None, :]).astype(
        jnp.int32
    )
    running = jnp.cumsum(onehot, axis=1) - 1
    position = jnp.sum(onehot * running, axis=2)
    slot_index = chosen * capacity + position
    pair_slot = slot_index[:, :, None] == jnp.arange(slot_count, dtype=jnp.int32)[None, None, :]
    token_slot = pair_slot.reshape(mbatch, tok_rows, top_count, slot_count).any(axis=2)
    token_slot = token_slot.astype(jnp.bfloat16)
    weight_pairs = route_weight[0].reshape(mbatch, pair_count)
    slot_weight = jnp.sum(jnp.where(pair_slot, weight_pairs[:, :, None], 0.0), axis=1)

    def to_slots(rows):
        gathered = jnp.einsum(
            "mts,mtd->msd", token_slot, rows, preferred_element_type=jnp.float32
        )
        return gathered

    def by_expert(slots):
        return (
            slots.reshape(mbatch, experts, capacity, model_width)
            .transpose(1, 0, 2, 3)
            .reshape(experts, mbatch * capacity, model_width)
        )

    input_slots = by_expert(to_slots(tokens).astype(jnp.bfloat16))
    sent_inputs = lax.all_to_all(input_slots, "expert", 0, 0, tiled=True)
    recv_inputs = lax.all_gather(sent_inputs, "dp", axis=0, tiled=True)

    scaled_slots = by_expert(
        (slot_weight[:, :, None] * to_slots(upstream)).astype(jnp.bfloat16)
    )
    sent_scaled = lax.all_to_all(scaled_slots, "expert", 0, 0, tiled=True)
    recv_scaled = lax.all_gather(sent_scaled, "dp", axis=0, tiled=True)

    input_rows = recv_inputs.reshape(-1, model_width)
    scaled_rows = recv_scaled.reshape(-1, model_width)
    gate_slice = w_gate[0, 0]
    up_slice = w_up[0, 0]
    down_slice = w_down[0, 0]
    partial_rows, gate_total, up_total, down_total = slice_backward(
        input_rows, scaled_rows, gate_slice, up_slice, down_slice
    )
    sent_back = partial_rows.astype(jnp.bfloat16).reshape(recv_inputs.shape)
    summed = lax.psum_scatter(sent_back, "dp", scatter_dimension=0, tiled=True)
    returned = lax.all_to_all(summed, "expert", 0, 0, tiled=True)
    back_slots = (
        returned.reshape(experts, mbatch, capacity, model_width)
        .transpose(1, 0, 2, 3)
        .reshape(mbatch, slot_count, model_width)
    )
    pair_sum = jnp.einsum(
        "mts,msd->mtd", token_slot, back_slots, preferred_element_type=jnp.float32
    )
    input_grad = (upstream.astype(jnp.float32) + pair_sum).astype(jnp.bfloat16)
    grad_gate = gate_total.astype(jnp.bfloat16)[None, None]
    grad_up = up_total.astype(jnp.bfloat16)[None, None]
    grad_down = down_total.astype(jnp.bfloat16)[None, None]
    return (input_grad[None], grad_gate, grad_up, grad_down)


def solution(mesh):
    return jax.shard_map(
        per_device,
        mesh=mesh,
        in_specs=(
            P("section", None, ("dp", "expert"), None),
            P("section", None, ("dp", "expert"), None),
            P("section", None, ("dp", "expert"), None),
            P("section", None, ("dp", "expert"), None),
            P("section", "expert", None, "dp"),
            P("section", "expert", None, "dp"),
            P("section", "expert", "dp", None),
        ),
        out_specs=(
            P("section", None, ("dp", "expert"), None),
            P("section", "expert", None, "dp"),
            P("section", "expert", None, "dp"),
            P("section", "expert", "dp", None),
        ),
        check_vma=False,
    )
```

```python
import jax
import jax.numpy as jnp
from jax import lax
from jax.sharding import PartitionSpec as P


def passed_along(x, axis, by):
    length = lax.axis_size(axis)
    return lax.ppermute(x, axis, [(i, (i + by) % length) for i in range(length)])


def slice_backward(pair_inputs, pair_scaled, gate_slice, up_slice, down_slice):
    contract_rows = (((0,), (0,)), ((), ()))
    contract_last = (((1,), (1,)), ((), ()))
    gate_pre = jnp.dot(pair_inputs, gate_slice, preferred_element_type=jnp.float32)
    up_pre = jnp.dot(pair_inputs, up_slice, preferred_element_type=jnp.float32)
    logistic = jax.nn.sigmoid(gate_pre)
    activated = gate_pre * logistic
    hidden = (activated * up_pre).astype(jnp.bfloat16)
    hidden_grad = lax.dot_general(
        pair_scaled, down_slice, contract_last, preferred_element_type=jnp.float32
    )
    gate_grad = (hidden_grad * up_pre * logistic * (1.0 + gate_pre * (1.0 - logistic))).astype(
        jnp.bfloat16
    )
    up_grad = (hidden_grad * activated).astype(jnp.bfloat16)
    down_total = lax.dot_general(
        hidden, pair_scaled, contract_rows, preferred_element_type=jnp.float32
    )
    gate_total = lax.dot_general(
        pair_inputs, gate_grad, contract_rows, preferred_element_type=jnp.float32
    )
    up_total = lax.dot_general(
        pair_inputs, up_grad, contract_rows, preferred_element_type=jnp.float32
    )
    partial_back = lax.dot_general(
        gate_grad, gate_slice, contract_last, preferred_element_type=jnp.float32
    )
    partial_back = partial_back + lax.dot_general(
        up_grad, up_slice, contract_last, preferred_element_type=jnp.float32
    )
    return (partial_back, gate_total, up_total, down_total)


def exchange(blocks, axis, sign):
    pieces = [blocks[0]]
    for shift in range(1, blocks.shape[0]):
        pieces.append(passed_along(blocks[shift], axis, sign * shift))
    return jnp.stack(pieces)


def per_device(incoming, stash, expert_ids, route_weight, w_gate, w_up, w_down):
    arrived = passed_along(incoming, "section", -1)
    upstream = arrived[0]
    tokens = stash[0]
    mbatch, tok_rows, model_width = tokens.shape
    top_count = expert_ids.shape[-1]
    experts = lax.axis_size("expert")
    capacity = max(2, 3 * tok_rows * top_count // (2 * experts))
    pair_count = tok_rows * top_count
    slot_count = experts * capacity
    block_rows = mbatch * capacity
    lanes = 128
    flat_rows = block_rows * model_width // lanes
    chosen = expert_ids[0].reshape(mbatch, pair_count)
    onehot = (chosen[:, :, None] == jnp.arange(experts, dtype=jnp.int32)[None, None, :]).astype(
        jnp.int32
    )
    running = jnp.cumsum(onehot, axis=1) - 1
    position = jnp.sum(onehot * running, axis=2)
    relative = (chosen - lax.axis_index("expert")) % experts
    slot_index = relative * capacity + position
    pair_slot = slot_index[:, :, None] == jnp.arange(slot_count, dtype=jnp.int32)[None, None, :]
    token_slot = pair_slot.reshape(mbatch, tok_rows, top_count, slot_count).any(axis=2)
    token_slot = token_slot.astype(jnp.bfloat16)
    weight_pairs = route_weight[0].reshape(mbatch, pair_count)
    slot_weight = jnp.sum(jnp.where(pair_slot, weight_pairs[:, :, None], 0.0), axis=1)

    def to_slots(rows):
        return jnp.einsum("mts,mtd->msd", token_slot, rows, preferred_element_type=jnp.float32)

    def by_expert(slots):
        return (
            slots.reshape(mbatch, experts, capacity, model_width)
            .transpose(1, 0, 2, 3)
            .reshape(experts, flat_rows, lanes)
        )

    def dispatch(slots):
        arrived_blocks = exchange(slots, "expert", 1)
        rows = arrived_blocks.reshape(experts * block_rows, model_width)
        rows = lax.all_gather(rows, "dpx", axis=0, tiled=True)
        return lax.all_gather(rows, "dpy", axis=0, tiled=True)

    input_rows = dispatch(by_expert(to_slots(tokens).astype(jnp.bfloat16)))
    scaled_rows = dispatch(
        by_expert((slot_weight[:, :, None] * to_slots(upstream)).astype(jnp.bfloat16))
    )
    gate_slice = w_gate[0, 0]
    up_slice = w_up[0, 0]
    down_slice = w_down[0, 0]
    partial_rows, gate_total, up_total, down_total = slice_backward(
        input_rows, scaled_rows, gate_slice, up_slice, down_slice
    )
    sent_back = partial_rows.astype(jnp.bfloat16)
    summed = lax.psum_scatter(sent_back, "dpy", scatter_dimension=0, tiled=True)
    summed = lax.psum_scatter(summed, "dpx", scatter_dimension=0, tiled=True)
    returned = exchange(summed.reshape(experts, flat_rows, lanes), "expert", -1)
    back_slots = (
        returned.reshape(experts, mbatch, capacity, model_width)
        .transpose(1, 0, 2, 3)
        .reshape(mbatch, slot_count, model_width)
    )
    pair_sum = jnp.einsum(
        "mts,msd->mtd", token_slot, back_slots, preferred_element_type=jnp.float32
    )
    input_grad = (upstream.astype(jnp.float32) + pair_sum).astype(jnp.bfloat16)
    grad_gate = gate_total.astype(jnp.bfloat16)[None, None]
    grad_up = up_total.astype(jnp.bfloat16)[None, None]
    grad_down = down_total.astype(jnp.bfloat16)[None, None]
    return (input_grad[None], grad_gate, grad_up, grad_down)


def solution(mesh):
    sections, replicas, experts = mesh.devices.shape
    split = jax.sharding.Mesh(
        mesh.devices.reshape(sections, replicas // 2, 2, experts),
        ("section", "dpy", "dpx", "expert"),
    )
    tokens = P("section", None, ("dpy", "dpx", "expert"), None)
    by_cols = P("section", "expert", None, ("dpy", "dpx"))
    by_rows = P("section", "expert", ("dpy", "dpx"), None)
    return jax.shard_map(
        per_device,
        mesh=split,
        in_specs=(tokens, tokens, tokens, tokens, by_cols, by_cols, by_rows),
        out_specs=(tokens, by_cols, by_cols, by_rows),
        check_vma=False,
    )
```

```python
import jax
import jax.numpy as jnp
from jax import lax
from jax.sharding import PartitionSpec as P


def passed_along(x, axis, by):
    length = lax.axis_size(axis)
    return lax.ppermute(x, axis, [(i, (i + by) % length) for i in range(length)])


def slice_backward(pair_inputs, pair_scaled, gate_slice, up_slice, down_slice):
    contract_rows = (((0,), (0,)), ((), ()))
    contract_last = (((1,), (1,)), ((), ()))
    gate_pre = jnp.dot(pair_inputs, gate_slice, preferred_element_type=jnp.float32)
    up_pre = jnp.dot(pair_inputs, up_slice, preferred_element_type=jnp.float32)
    logistic = jax.nn.sigmoid(gate_pre)
    activated = gate_pre * logistic
    hidden = (activated * up_pre).astype(jnp.bfloat16)
    hidden_grad = lax.dot_general(
        pair_scaled, down_slice, contract_last, preferred_element_type=jnp.float32
    )
    gate_grad = (hidden_grad * up_pre * logistic * (1.0 + gate_pre * (1.0 - logistic))).astype(
        jnp.bfloat16
    )
    up_grad = (hidden_grad * activated).astype(jnp.bfloat16)
    down_total = lax.dot_general(
        hidden, pair_scaled, contract_rows, preferred_element_type=jnp.float32
    )
    gate_total = lax.dot_general(
        pair_inputs, gate_grad, contract_rows, preferred_element_type=jnp.float32
    )
    up_total = lax.dot_general(
        pair_inputs, up_grad, contract_rows, preferred_element_type=jnp.float32
    )
    partial_back = lax.dot_general(
        gate_grad, gate_slice, contract_last, preferred_element_type=jnp.float32
    )
    partial_back = partial_back + lax.dot_general(
        up_grad, up_slice, contract_last, preferred_element_type=jnp.float32
    )
    return (partial_back, gate_total, up_total, down_total)


def exchange(blocks, axis, sign):
    pieces = [blocks[0]]
    for shift in range(1, blocks.shape[0]):
        pieces.append(passed_along(blocks[shift], axis, sign * shift))
    return jnp.stack(pieces)


def along_x(x, sign):
    sections = lax.axis_size("section")
    halves = lax.axis_size("dpx")
    pairs = []
    for section in range(sections):
        low = section // 2
        for half in range(halves):
            if (low == 0) == (sign > 0):
                target = (section + 2 if low == 0 else section - 2, half)
            else:
                target = (section - 2 if low == 1 else section + 2, (half + sign) % halves)
            pairs.append((section * halves + half, target[0] * halves + target[1]))
    return lax.ppermute(x, ("section", "dpx"), pairs)


def to_x_partner(x):
    cut = x.shape[0] // 2
    ahead = along_x(along_x(x[:cut], 1), 1)
    behind = along_x(along_x(x[cut:], -1), -1)
    return jnp.concatenate([ahead, behind], axis=0)


def per_device(incoming, stash, expert_ids, route_weight, w_gate, w_up, w_down):
    arrived = passed_along(incoming, "section", -1)
    upstream = arrived[0]
    tokens = stash[0]
    mbatch, tok_rows, model_width = tokens.shape
    top_count = expert_ids.shape[-1]
    experts = lax.axis_size("expert")
    capacity = max(2, 3 * tok_rows * top_count // (2 * experts))
    pair_count = tok_rows * top_count
    slot_count = experts * capacity
    block_rows = mbatch * capacity
    lanes = 128
    flat_rows = block_rows * model_width // lanes
    chosen = expert_ids[0].reshape(mbatch, pair_count)
    onehot = (chosen[:, :, None] == jnp.arange(experts, dtype=jnp.int32)[None, None, :]).astype(
        jnp.int32
    )
    running = jnp.cumsum(onehot, axis=1) - 1
    position = jnp.sum(onehot * running, axis=2)
    relative = (chosen - lax.axis_index("expert")) % experts
    slot_index = relative * capacity + position
    pair_slot = slot_index[:, :, None] == jnp.arange(slot_count, dtype=jnp.int32)[None, None, :]
    token_slot = pair_slot.reshape(mbatch, tok_rows, top_count, slot_count).any(axis=2)
    token_slot = token_slot.astype(jnp.bfloat16)
    weight_pairs = route_weight[0].reshape(mbatch, pair_count)
    slot_weight = jnp.sum(jnp.where(pair_slot, weight_pairs[:, :, None], 0.0), axis=1)

    def to_slots(rows):
        return jnp.einsum("mts,mtd->msd", token_slot, rows, preferred_element_type=jnp.float32)

    def by_expert(slots):
        return (
            slots.reshape(mbatch, experts, capacity, model_width)
            .transpose(1, 0, 2, 3)
            .reshape(experts, flat_rows, lanes)
        )

    def dispatch(slots):
        arrived_blocks = exchange(slots, "expert", 1)
        rows = arrived_blocks.reshape(experts * block_rows, model_width)
        rows = jnp.concatenate([rows, to_x_partner(rows)], axis=0)
        return lax.all_gather(rows, "dpy", axis=0, tiled=True)

    input_rows = dispatch(by_expert(to_slots(tokens).astype(jnp.bfloat16)))
    scaled_rows = dispatch(
        by_expert((slot_weight[:, :, None] * to_slots(upstream)).astype(jnp.bfloat16))
    )
    gate_slice = w_gate[0, 0]
    up_slice = w_up[0, 0]
    down_slice = w_down[0, 0]
    partial_rows, gate_total, up_total, down_total = slice_backward(
        input_rows, scaled_rows, gate_slice, up_slice, down_slice
    )
    sent_back = partial_rows.astype(jnp.bfloat16)
    summed = lax.psum_scatter(sent_back, "dpy", scatter_dimension=0, tiled=True)
    own_rows = summed.shape[0] // 2
    summed = (
        summed[:own_rows].astype(jnp.float32)
        + to_x_partner(summed[own_rows:]).astype(jnp.float32)
    ).astype(jnp.bfloat16)
    returned = exchange(summed.reshape(experts, flat_rows, lanes), "expert", -1)
    back_slots = (
        returned.reshape(experts, mbatch, capacity, model_width)
        .transpose(1, 0, 2, 3)
        .reshape(mbatch, slot_count, model_width)
    )
    pair_sum = jnp.einsum(
        "mts,msd->mtd", token_slot, back_slots, preferred_element_type=jnp.float32
    )
    input_grad = (upstream.astype(jnp.float32) + pair_sum).astype(jnp.bfloat16)
    grad_gate = gate_total.astype(jnp.bfloat16)[None, None]
    grad_up = up_total.astype(jnp.bfloat16)[None, None]
    grad_down = down_total.astype(jnp.bfloat16)[None, None]
    return (input_grad[None], grad_gate, grad_up, grad_down)


def solution(mesh):
    sections, replicas, experts = mesh.devices.shape
    split = jax.sharding.Mesh(
        mesh.devices.reshape(sections, replicas // 2, 2, experts),
        ("section", "dpy", "dpx", "expert"),
    )
    tokens = P("section", None, ("dpy", "dpx", "expert"), None)
    by_cols = P("section", "expert", None, ("dpy", "dpx"))
    by_rows = P("section", "expert", ("dpy", "dpx"), None)
    return jax.shard_map(
        per_device,
        mesh=split,
        in_specs=(tokens, tokens, tokens, tokens, by_cols, by_cols, by_rows),
        out_specs=(tokens, by_cols, by_cols, by_rows),
        check_vma=False,
    )
```

```python
import jax
import jax.numpy as jnp
from jax import lax
from jax.sharding import PartitionSpec as P


def passed_along(x, axis, by):
    length = lax.axis_size(axis)
    return lax.ppermute(x, axis, [(i, (i + by) % length) for i in range(length)])


def slice_backward(pair_inputs, pair_scaled, gate_slice, up_slice, down_slice):
    contract_rows = (((0,), (0,)), ((), ()))
    contract_last = (((1,), (1,)), ((), ()))
    gate_pre = jnp.dot(pair_inputs, gate_slice, preferred_element_type=jnp.float32)
    up_pre = jnp.dot(pair_inputs, up_slice, preferred_element_type=jnp.float32)
    logistic = jax.nn.sigmoid(gate_pre)
    activated = gate_pre * logistic
    hidden = (activated * up_pre).astype(jnp.bfloat16)
    hidden_grad = lax.dot_general(
        pair_scaled, down_slice, contract_last, preferred_element_type=jnp.float32
    )
    gate_grad = (hidden_grad * up_pre * logistic * (1.0 + gate_pre * (1.0 - logistic))).astype(
        jnp.bfloat16
    )
    up_grad = (hidden_grad * activated).astype(jnp.bfloat16)
    down_total = lax.dot_general(
        hidden, pair_scaled, contract_rows, preferred_element_type=jnp.float32
    )
    gate_total = lax.dot_general(
        pair_inputs, gate_grad, contract_rows, preferred_element_type=jnp.float32
    )
    up_total = lax.dot_general(
        pair_inputs, up_grad, contract_rows, preferred_element_type=jnp.float32
    )
    partial_back = lax.dot_general(
        gate_grad, gate_slice, contract_last, preferred_element_type=jnp.float32
    )
    partial_back = partial_back + lax.dot_general(
        up_grad, up_slice, contract_last, preferred_element_type=jnp.float32
    )
    return (partial_back, gate_total, up_total, down_total)


def along_x(x, sign):
    sections = lax.axis_size("section")
    halves = lax.axis_size("dpx")
    pairs = []
    for section in range(sections):
        low = section // 2
        for half in range(halves):
            if (low == 0) == (sign > 0):
                target = (section + 2 if low == 0 else section - 2, half)
            else:
                target = (section - 2 if low == 1 else section + 2, (half + sign) % halves)
            pairs.append((section * halves + half, target[0] * halves + target[1]))
    return lax.ppermute(x, ("section", "dpx"), pairs)


def to_x_partner(x):
    cut = x.shape[1] // 2
    ahead = along_x(along_x(x[:, :cut], 1), 1)
    behind = along_x(along_x(x[:, cut:], -1), -1)
    return jnp.concatenate([ahead, behind], axis=1)


def per_device(incoming, stash, expert_ids, route_weight, w_gate, w_up, w_down):
    arrived = passed_along(incoming, "section", -1)
    upstream = arrived[0]
    tokens = stash[0]
    mbatch, tok_rows, model_width = tokens.shape
    top_count = expert_ids.shape[-1]
    experts = lax.axis_size("expert")
    capacity = max(2, 3 * tok_rows * top_count // (2 * experts))
    pair_count = tok_rows * top_count
    slot_count = experts * capacity
    block_rows = mbatch * capacity
    lanes = 128
    flat_rows = block_rows * model_width // lanes
    chosen = expert_ids[0].reshape(mbatch, pair_count)
    onehot = (chosen[:, :, None] == jnp.arange(experts, dtype=jnp.int32)[None, None, :]).astype(
        jnp.int32
    )
    running = jnp.cumsum(onehot, axis=1) - 1
    position = jnp.sum(onehot * running, axis=2)
    relative = (chosen - lax.axis_index("expert")) % experts
    slot_index = relative * capacity + position
    pair_slot = slot_index[:, :, None] == jnp.arange(slot_count, dtype=jnp.int32)[None, None, :]
    token_slot = pair_slot.reshape(mbatch, tok_rows, top_count, slot_count).any(axis=2)
    token_slot = token_slot.astype(jnp.bfloat16)
    weight_pairs = route_weight[0].reshape(mbatch, pair_count)
    slot_weight = jnp.sum(jnp.where(pair_slot, weight_pairs[:, :, None], 0.0), axis=1)

    def to_slots(rows):
        return jnp.einsum("mts,mtd->msd", token_slot, rows, preferred_element_type=jnp.float32)

    def by_expert(slots):
        return (
            slots.reshape(mbatch, experts, capacity, model_width)
            .transpose(1, 0, 2, 3)
            .reshape(experts, flat_rows, lanes)
        )

    def dispatch(slots, first):
        pieces = [
            slots[s] if first + s == 0 else passed_along(slots[s], "expert", first + s)
            for s in range(slots.shape[0])
        ]
        rows = jnp.stack(pieces).reshape(-1, model_width)
        rows = jnp.concatenate([rows, to_x_partner(rows)], axis=0)
        return lax.all_gather(rows, "dpy", axis=0, tiled=True)

    def give_back(partials, first):
        summed = lax.psum_scatter(partials, "dpy", scatter_dimension=0, tiled=True)
        own_rows = summed.shape[0] // 2
        summed = (
            summed[:own_rows].astype(jnp.float32)
            + to_x_partner(summed[own_rows:]).astype(jnp.float32)
        ).astype(jnp.bfloat16)
        blocks = summed.reshape(-1, flat_rows, lanes)
        pieces = [
            blocks[s] if first + s == 0 else passed_along(blocks[s], "expert", -(first + s))
            for s in range(blocks.shape[0])
        ]
        return jnp.stack(pieces)

    input_slots = by_expert(to_slots(tokens).astype(jnp.bfloat16))
    scaled_slots = by_expert(
        (slot_weight[:, :, None] * to_slots(upstream)).astype(jnp.bfloat16)
    )
    gate_slice = w_gate[0, 0]
    up_slice = w_up[0, 0]
    down_slice = w_down[0, 0]
    chunks = 2
    per_chunk = experts // chunks
    totals = None
    returned = []
    for chunk in range(chunks):
        first = chunk * per_chunk
        input_rows = dispatch(input_slots[first:first + per_chunk], first)
        scaled_rows = dispatch(scaled_slots[first:first + per_chunk], first)
        partial_rows, *sums = slice_backward(
            input_rows, scaled_rows, gate_slice, up_slice, down_slice
        )
        totals = sums if totals is None else [a + b for a, b in zip(totals, sums)]
        returned.append(give_back(partial_rows.astype(jnp.bfloat16), first))
    gate_total, up_total, down_total = totals
    returned = jnp.concatenate(returned, axis=0)
    back_slots = (
        returned.reshape(experts, mbatch, capacity, model_width)
        .transpose(1, 0, 2, 3)
        .reshape(mbatch, slot_count, model_width)
    )
    pair_sum = jnp.einsum(
        "mts,msd->mtd", token_slot, back_slots, preferred_element_type=jnp.float32
    )
    input_grad = (upstream.astype(jnp.float32) + pair_sum).astype(jnp.bfloat16)
    grad_gate = gate_total.astype(jnp.bfloat16)[None, None]
    grad_up = up_total.astype(jnp.bfloat16)[None, None]
    grad_down = down_total.astype(jnp.bfloat16)[None, None]
    return (input_grad[None], grad_gate, grad_up, grad_down)


def solution(mesh):
    sections, replicas, experts = mesh.devices.shape
    split = jax.sharding.Mesh(
        mesh.devices.reshape(sections, replicas // 2, 2, experts),
        ("section", "dpy", "dpx", "expert"),
    )
    tokens = P("section", None, ("dpy", "dpx", "expert"), None)
    by_cols = P("section", "expert", None, ("dpy", "dpx"))
    by_rows = P("section", "expert", ("dpy", "dpx"), None)
    return jax.shard_map(
        per_device,
        mesh=split,
        in_specs=(tokens, tokens, tokens, tokens, by_cols, by_cols, by_rows),
        out_specs=(tokens, by_cols, by_cols, by_rows),
        check_vma=False,
    )
```

```python
import jax
import jax.numpy as jnp
from jax import lax
from jax.sharding import PartitionSpec as P


def passed_along(x, axis, by):
    length = lax.axis_size(axis)
    return lax.ppermute(x, axis, [(i, (i + by) % length) for i in range(length)])


def slice_backward(pair_inputs, pair_scaled, gate_slice, up_slice, down_slice):
    contract_rows = (((0,), (0,)), ((), ()))
    contract_last = (((1,), (1,)), ((), ()))
    gate_pre = jnp.dot(pair_inputs, gate_slice, preferred_element_type=jnp.float32)
    up_pre = jnp.dot(pair_inputs, up_slice, preferred_element_type=jnp.float32)
    logistic = jax.nn.sigmoid(gate_pre)
    activated = gate_pre * logistic
    hidden = (activated * up_pre).astype(jnp.bfloat16)
    hidden_grad = lax.dot_general(
        pair_scaled, down_slice, contract_last, preferred_element_type=jnp.float32
    )
    gate_grad = (hidden_grad * up_pre * logistic * (1.0 + gate_pre * (1.0 - logistic))).astype(
        jnp.bfloat16
    )
    up_grad = (hidden_grad * activated).astype(jnp.bfloat16)
    down_total = lax.dot_general(
        hidden, pair_scaled, contract_rows, preferred_element_type=jnp.float32
    )
    gate_total = lax.dot_general(
        pair_inputs, gate_grad, contract_rows, preferred_element_type=jnp.float32
    )
    up_total = lax.dot_general(
        pair_inputs, up_grad, contract_rows, preferred_element_type=jnp.float32
    )
    partial_back = lax.dot_general(
        gate_grad, gate_slice, contract_last, preferred_element_type=jnp.float32
    )
    partial_back = partial_back + lax.dot_general(
        up_grad, up_slice, contract_last, preferred_element_type=jnp.float32
    )
    return (partial_back, gate_total, up_total, down_total)


def exchange(blocks, axis, sign):
    pieces = [blocks[0]]
    for shift in range(1, blocks.shape[0]):
        pieces.append(passed_along(blocks[shift], axis, sign * shift))
    return jnp.stack(pieces)


def along_x(x, sign):
    sections = lax.axis_size("section")
    halves = lax.axis_size("dpx")
    pairs = []
    for section in range(sections):
        low = section // 2
        for half in range(halves):
            if (low == 0) == (sign > 0):
                target = (section + 2 if low == 0 else section - 2, half)
            else:
                target = (section - 2 if low == 1 else section + 2, (half + sign) % halves)
            pairs.append((section * halves + half, target[0] * halves + target[1]))
    return lax.ppermute(x, ("section", "dpx"), pairs)


def to_x_partner(x):
    cut = x.shape[1] // 2
    ahead = along_x(along_x(x[:, :cut], 1), 1)
    behind = along_x(along_x(x[:, cut:], -1), -1)
    return jnp.concatenate([ahead, behind], axis=1)


def per_device(incoming, stash, expert_ids, route_weight, w_gate, w_up, w_down):
    arrived = passed_along(incoming, "section", -1)
    upstream = arrived[0]
    tokens = stash[0]
    mbatch, tok_rows, model_width = tokens.shape
    top_count = expert_ids.shape[-1]
    experts = lax.axis_size("expert")
    capacity = max(2, 3 * tok_rows * top_count // (2 * experts))
    pair_count = tok_rows * top_count
    slot_count = experts * capacity
    block_rows = mbatch * capacity
    lanes = 128
    flat_rows = block_rows * model_width // lanes
    chosen = expert_ids[0].reshape(mbatch, pair_count)
    onehot = (chosen[:, :, None] == jnp.arange(experts, dtype=jnp.int32)[None, None, :]).astype(
        jnp.int32
    )
    running = jnp.cumsum(onehot, axis=1) - 1
    position = jnp.sum(onehot * running, axis=2)
    relative = (chosen - lax.axis_index("expert")) % experts
    slot_index = relative * capacity + position
    pair_slot = slot_index[:, :, None] == jnp.arange(slot_count, dtype=jnp.int32)[None, None, :]
    token_slot = pair_slot.reshape(mbatch, tok_rows, top_count, slot_count).any(axis=2)
    token_slot = token_slot.astype(jnp.bfloat16)
    weight_pairs = route_weight[0].reshape(mbatch, pair_count)
    slot_weight = jnp.sum(jnp.where(pair_slot, weight_pairs[:, :, None], 0.0), axis=1)

    def to_slots(rows):
        return jnp.einsum("mts,mtd->msd", token_slot, rows, preferred_element_type=jnp.float32)

    both_slots = jnp.stack(
        [
            to_slots(tokens).astype(jnp.bfloat16),
            (slot_weight[:, :, None] * to_slots(upstream)).astype(jnp.bfloat16),
        ]
    )
    both_slots = (
        both_slots.reshape(2, mbatch, experts, capacity, model_width)
        .transpose(2, 0, 1, 3, 4)
        .reshape(experts, 2 * flat_rows, lanes)
    )
    arrived_blocks = exchange(both_slots, "expert", 1)
    both_rows = (
        arrived_blocks.reshape(experts, 2, block_rows, model_width)
        .transpose(1, 0, 2, 3)
        .reshape(2 * experts * block_rows, model_width)
    )
    partner_rows = to_x_partner(both_rows)
    local_rows = experts * block_rows

    def gathered(part):
        own = both_rows[part * local_rows:(part + 1) * local_rows]
        partner = partner_rows[part * local_rows:(part + 1) * local_rows]
        rows = jnp.concatenate([own, partner], axis=0)
        return lax.all_gather(rows, "dpy", axis=0, tiled=True)

    input_rows = gathered(0)
    scaled_rows = gathered(1)
    gate_slice = w_gate[0, 0]
    up_slice = w_up[0, 0]
    down_slice = w_down[0, 0]
    partial_rows, gate_total, up_total, down_total = slice_backward(
        input_rows, scaled_rows, gate_slice, up_slice, down_slice
    )
    sent_back = partial_rows.astype(jnp.bfloat16)
    summed = lax.psum_scatter(sent_back, "dpy", scatter_dimension=0, tiled=True)
    own_rows = summed.shape[0] // 2
    summed = (
        summed[:own_rows].astype(jnp.float32)
        + to_x_partner(summed[own_rows:]).astype(jnp.float32)
    ).astype(jnp.bfloat16)
    returned = exchange(summed.reshape(experts, flat_rows, lanes), "expert", -1)
    back_slots = (
        returned.reshape(experts, mbatch, capacity, model_width)
        .transpose(1, 0, 2, 3)
        .reshape(mbatch, slot_count, model_width)
    )
    pair_sum = jnp.einsum(
        "mts,msd->mtd", token_slot, back_slots, preferred_element_type=jnp.float32
    )
    input_grad = (upstream.astype(jnp.float32) + pair_sum).astype(jnp.bfloat16)
    grad_gate = gate_total.astype(jnp.bfloat16)[None, None]
    grad_up = up_total.astype(jnp.bfloat16)[None, None]
    grad_down = down_total.astype(jnp.bfloat16)[None, None]
    return (input_grad[None], grad_gate, grad_up, grad_down)


def solution(mesh):
    sections, replicas, experts = mesh.devices.shape
    split = jax.sharding.Mesh(
        mesh.devices.reshape(sections, replicas // 2, 2, experts),
        ("section", "dpy", "dpx", "expert"),
    )
    tokens = P("section", None, ("dpy", "dpx", "expert"), None)
    by_cols = P("section", "expert", None, ("dpy", "dpx"))
    by_rows = P("section", "expert", ("dpy", "dpx"), None)
    return jax.shard_map(
        per_device,
        mesh=split,
        in_specs=(tokens, tokens, tokens, tokens, by_cols, by_cols, by_rows),
        out_specs=(tokens, by_cols, by_cols, by_rows),
        check_vma=False,
    )
```

```python
import jax
import jax.numpy as jnp
from jax import lax
from jax.sharding import PartitionSpec as P


def passed_along(x, axis, by):
    length = lax.axis_size(axis)
    return lax.ppermute(x, axis, [(i, (i + by) % length) for i in range(length)])


def slice_backward(pair_inputs, pair_scaled, gate_slice, up_slice, down_slice):
    contract_rows = (((0,), (0,)), ((), ()))
    contract_last = (((1,), (1,)), ((), ()))
    gate_pre = jnp.dot(pair_inputs, gate_slice, preferred_element_type=jnp.float32)
    up_pre = jnp.dot(pair_inputs, up_slice, preferred_element_type=jnp.float32)
    logistic = jax.nn.sigmoid(gate_pre)
    activated = gate_pre * logistic
    hidden = (activated * up_pre).astype(jnp.bfloat16)
    hidden_grad = lax.dot_general(
        pair_scaled, down_slice, contract_last, preferred_element_type=jnp.float32
    )
    gate_grad = (hidden_grad * up_pre * logistic * (1.0 + gate_pre * (1.0 - logistic))).astype(
        jnp.bfloat16
    )
    up_grad = (hidden_grad * activated).astype(jnp.bfloat16)
    down_total = lax.dot_general(
        hidden, pair_scaled, contract_rows, preferred_element_type=jnp.float32
    )
    gate_total = lax.dot_general(
        pair_inputs, gate_grad, contract_rows, preferred_element_type=jnp.float32
    )
    up_total = lax.dot_general(
        pair_inputs, up_grad, contract_rows, preferred_element_type=jnp.float32
    )
    partial_back = lax.dot_general(
        gate_grad, gate_slice, contract_last, preferred_element_type=jnp.float32
    )
    partial_back = partial_back + lax.dot_general(
        up_grad, up_slice, contract_last, preferred_element_type=jnp.float32
    )
    return (partial_back, gate_total, up_total, down_total)


def exchange(blocks, axis, sign):
    pieces = [blocks[0]]
    for shift in range(1, blocks.shape[0]):
        pieces.append(passed_along(blocks[shift], axis, sign * shift))
    return jnp.stack(pieces)


def across_x(x, shift):
    halves = lax.axis_size("dpx")
    experts = lax.axis_size("expert")
    pairs = [
        (half * experts + e, (1 - half) * experts + (e + shift) % experts)
        for half in range(halves)
        for e in range(experts)
    ]
    return lax.ppermute(x, ("dpx", "expert"), pairs)


def per_device(incoming, stash, expert_ids, route_weight, w_gate, w_up, w_down):
    arrived = passed_along(incoming, "section", -1)
    upstream = arrived[0]
    tokens = stash[0]
    mbatch, tok_rows, model_width = tokens.shape
    top_count = expert_ids.shape[-1]
    experts = lax.axis_size("expert")
    capacity = max(2, 3 * tok_rows * top_count // (2 * experts))
    pair_count = tok_rows * top_count
    slot_count = experts * capacity
    block_rows = mbatch * capacity
    lanes = 128
    flat_rows = block_rows * model_width // lanes
    chosen = expert_ids[0].reshape(mbatch, pair_count)
    onehot = (chosen[:, :, None] == jnp.arange(experts, dtype=jnp.int32)[None, None, :]).astype(
        jnp.int32
    )
    running = jnp.cumsum(onehot, axis=1) - 1
    position = jnp.sum(onehot * running, axis=2)
    relative = (chosen - lax.axis_index("expert")) % experts
    slot_index = relative * capacity + position
    pair_slot = slot_index[:, :, None] == jnp.arange(slot_count, dtype=jnp.int32)[None, None, :]
    token_slot = pair_slot.reshape(mbatch, tok_rows, top_count, slot_count).any(axis=2)
    token_slot = token_slot.astype(jnp.bfloat16)
    weight_pairs = route_weight[0].reshape(mbatch, pair_count)
    slot_weight = jnp.sum(jnp.where(pair_slot, weight_pairs[:, :, None], 0.0), axis=1)

    def to_slots(rows):
        return jnp.einsum("mts,mtd->msd", token_slot, rows, preferred_element_type=jnp.float32)

    def by_expert(slots):
        return (
            slots.reshape(mbatch, experts, capacity, model_width)
            .transpose(1, 0, 2, 3)
            .reshape(experts, flat_rows, lanes)
        )

    def dispatch(slots):
        own = exchange(slots, "expert", 1)
        other = jnp.stack([across_x(slots[shift], shift) for shift in range(experts)])
        rows = jnp.concatenate([own, other], axis=0).reshape(-1, model_width)
        return lax.all_gather(rows, "dpy", axis=0, tiled=True)

    input_rows = dispatch(by_expert(to_slots(tokens).astype(jnp.bfloat16)))
    scaled_rows = dispatch(
        by_expert((slot_weight[:, :, None] * to_slots(upstream)).astype(jnp.bfloat16))
    )
    gate_slice = w_gate[0, 0]
    up_slice = w_up[0, 0]
    down_slice = w_down[0, 0]
    partial_rows, gate_total, up_total, down_total = slice_backward(
        input_rows, scaled_rows, gate_slice, up_slice, down_slice
    )
    sent_back = partial_rows.astype(jnp.bfloat16)
    summed = lax.psum_scatter(sent_back, "dpy", scatter_dimension=0, tiled=True)
    summed = summed.reshape(2, experts, flat_rows, lanes)
    own_back = exchange(summed[0], "expert", -1)
    other_back = jnp.stack([across_x(summed[1, shift], -shift) for shift in range(experts)])

    def to_tokens(blocks):
        back_slots = (
            blocks.reshape(experts, mbatch, capacity, model_width)
            .transpose(1, 0, 2, 3)
            .reshape(mbatch, slot_count, model_width)
        )
        return jnp.einsum(
            "mts,msd->mtd", token_slot, back_slots, preferred_element_type=jnp.float32
        )

    pair_sum = to_tokens(own_back) + to_tokens(other_back)
    input_grad = (upstream.astype(jnp.float32) + pair_sum).astype(jnp.bfloat16)
    grad_gate = gate_total.astype(jnp.bfloat16)[None, None]
    grad_up = up_total.astype(jnp.bfloat16)[None, None]
    grad_down = down_total.astype(jnp.bfloat16)[None, None]
    return (input_grad[None], grad_gate, grad_up, grad_down)


def solution(mesh):
    sections, replicas, experts = mesh.devices.shape
    split = jax.sharding.Mesh(
        mesh.devices.reshape(sections, replicas // 2, 2, experts),
        ("section", "dpy", "dpx", "expert"),
    )
    tokens = P("section", None, ("dpy", "dpx", "expert"), None)
    by_cols = P("section", "expert", None, ("dpy", "dpx"))
    by_rows = P("section", "expert", ("dpy", "dpx"), None)
    return jax.shard_map(
        per_device,
        mesh=split,
        in_specs=(tokens, tokens, tokens, tokens, by_cols, by_cols, by_rows),
        out_specs=(tokens, by_cols, by_cols, by_rows),
        check_vma=False,
    )
```

```python
import jax
import jax.numpy as jnp
from jax import lax
from jax.sharding import PartitionSpec as P


def passed_along(x, axis, by):
    length = lax.axis_size(axis)
    return lax.ppermute(x, axis, [(i, (i + by) % length) for i in range(length)])


def slice_backward(pair_inputs, pair_scaled, gate_slice, up_slice, down_slice):
    contract_rows = (((0,), (0,)), ((), ()))
    contract_last = (((1,), (1,)), ((), ()))
    gate_pre = jnp.dot(pair_inputs, gate_slice, preferred_element_type=jnp.float32)
    up_pre = jnp.dot(pair_inputs, up_slice, preferred_element_type=jnp.float32)
    logistic = jax.nn.sigmoid(gate_pre)
    activated = gate_pre * logistic
    hidden = (activated * up_pre).astype(jnp.bfloat16)
    hidden_grad = lax.dot_general(
        pair_scaled, down_slice, contract_last, preferred_element_type=jnp.float32
    )
    gate_grad = (hidden_grad * up_pre * logistic * (1.0 + gate_pre * (1.0 - logistic))).astype(
        jnp.bfloat16
    )
    up_grad = (hidden_grad * activated).astype(jnp.bfloat16)
    down_total = lax.dot_general(
        hidden, pair_scaled, contract_rows, preferred_element_type=jnp.float32
    )
    gate_total = lax.dot_general(
        pair_inputs, gate_grad, contract_rows, preferred_element_type=jnp.float32
    )
    up_total = lax.dot_general(
        pair_inputs, up_grad, contract_rows, preferred_element_type=jnp.float32
    )
    partial_back = lax.dot_general(
        gate_grad, gate_slice, contract_last, preferred_element_type=jnp.float32
    )
    partial_back = partial_back + lax.dot_general(
        up_grad, up_slice, contract_last, preferred_element_type=jnp.float32
    )
    return (partial_back, gate_total, up_total, down_total)


def exchange(blocks, axis, sign):
    pieces = [blocks[0]]
    for shift in range(1, blocks.shape[0]):
        pieces.append(passed_along(blocks[shift], axis, sign * shift))
    return jnp.stack(pieces)


def along_x(x, sign):
    sections = lax.axis_size("section")
    halves = lax.axis_size("dpx")
    pairs = []
    for section in range(sections):
        low = section // 2
        for half in range(halves):
            if (low == 0) == (sign > 0):
                target = (section + 2 if low == 0 else section - 2, half)
            else:
                target = (section - 2 if low == 1 else section + 2, (half + sign) % halves)
            pairs.append((section * halves + half, target[0] * halves + target[1]))
    return lax.ppermute(x, ("section", "dpx"), pairs)


def to_x_partner(x):
    cut = x.shape[0] // 2
    ahead = along_x(along_x(x[:cut], 1), 1)
    behind = along_x(along_x(x[cut:], -1), -1)
    return jnp.concatenate([ahead, behind], axis=0)


def per_device(incoming, stash, expert_ids, route_weight, w_gate, w_up, w_down):
    arrived = passed_along(incoming, "section", -1)
    upstream = arrived[0]
    tokens = stash[0]
    mbatch, tok_rows, model_width = tokens.shape
    top_count = expert_ids.shape[-1]
    experts = lax.axis_size("expert")
    capacity = max(2, 3 * tok_rows * top_count // (2 * experts))
    pair_count = tok_rows * top_count
    slot_count = experts * capacity
    block_rows = mbatch * capacity
    lanes = 128
    flat_rows = block_rows * model_width // lanes
    chosen = expert_ids[0].reshape(mbatch, pair_count)
    onehot = (chosen[:, :, None] == jnp.arange(experts, dtype=jnp.int32)[None, None, :]).astype(
        jnp.int32
    )
    running = jnp.cumsum(onehot, axis=1) - 1
    position = jnp.sum(onehot * running, axis=2)
    relative = (chosen - lax.axis_index("expert")) % experts
    slot_index = relative * capacity + position
    pair_slot = slot_index[:, :, None] == jnp.arange(slot_count, dtype=jnp.int32)[None, None, :]
    token_slot = pair_slot.reshape(mbatch, tok_rows, top_count, slot_count).any(axis=2)
    token_slot = token_slot.astype(jnp.bfloat16)
    weight_pairs = route_weight[0].reshape(mbatch, pair_count)
    slot_weight = jnp.sum(jnp.where(pair_slot, weight_pairs[:, :, None], 0.0), axis=1)

    def to_slots(rows):
        return jnp.einsum("mts,mtd->msd", token_slot, rows, preferred_element_type=jnp.float32)

    def by_expert(slots):
        return (
            slots.reshape(mbatch, experts, capacity, model_width)
            .transpose(1, 0, 2, 3)
            .reshape(experts, flat_rows, lanes)
        )

    def dispatch(slots):
        arrived_blocks = exchange(slots, "expert", 1)
        rows = arrived_blocks.reshape(experts * block_rows, model_width)
        rows = jnp.concatenate([rows, to_x_partner(rows)], axis=0)
        return lax.all_gather(rows, "dpy", axis=0, tiled=True)

    input_rows = dispatch(by_expert(to_slots(tokens).astype(jnp.bfloat16)))
    scaled_rows = dispatch(
        by_expert((slot_weight[:, :, None] * to_slots(upstream)).astype(jnp.bfloat16))
    )
    gate_slice = w_gate[0, 0]
    up_slice = w_up[0, 0]
    down_slice = w_down[0, 0]
    partial_rows, gate_total, up_total, down_total = slice_backward(
        input_rows, scaled_rows, gate_slice, up_slice, down_slice
    )
    sent_back = partial_rows.astype(jnp.bfloat16)
    summed = lax.psum_scatter(sent_back, "dpy", scatter_dimension=0, tiled=True)
    own_rows = summed.shape[0] // 2
    summed = (
        summed[:own_rows].astype(jnp.float32)
        + to_x_partner(summed[own_rows:]).astype(jnp.float32)
    ).astype(jnp.bfloat16)
    here = lax.axis_index("expert")
    blocks = summed.reshape(experts, flat_rows, lanes)
    flipped = jnp.concatenate([blocks[:1], blocks[1:][::-1]], axis=0)
    by_source = jnp.roll(flipped, here, axis=0)
    by_expert_device = lax.all_to_all(by_source, "expert", 0, 0, tiled=True)
    returned = jnp.roll(by_expert_device, -here, axis=0)
    back_slots = (
        returned.reshape(experts, mbatch, capacity, model_width)
        .transpose(1, 0, 2, 3)
        .reshape(mbatch, slot_count, model_width)
    )
    pair_sum = jnp.einsum(
        "mts,msd->mtd", token_slot, back_slots, preferred_element_type=jnp.float32
    )
    input_grad = (upstream.astype(jnp.float32) + pair_sum).astype(jnp.bfloat16)
    grad_gate = gate_total.astype(jnp.bfloat16)[None, None]
    grad_up = up_total.astype(jnp.bfloat16)[None, None]
    grad_down = down_total.astype(jnp.bfloat16)[None, None]
    return (input_grad[None], grad_gate, grad_up, grad_down)


def solution(mesh):
    sections, replicas, experts = mesh.devices.shape
    split = jax.sharding.Mesh(
        mesh.devices.reshape(sections, replicas // 2, 2, experts),
        ("section", "dpy", "dpx", "expert"),
    )
    tokens = P("section", None, ("dpy", "dpx", "expert"), None)
    by_cols = P("section", "expert", None, ("dpy", "dpx"))
    by_rows = P("section", "expert", ("dpy", "dpx"), None)
    return jax.shard_map(
        per_device,
        mesh=split,
        in_specs=(tokens, tokens, tokens, tokens, by_cols, by_cols, by_rows),
        out_specs=(tokens, by_cols, by_cols, by_rows),
        check_vma=False,
    )
```

```python
import jax
import jax.numpy as jnp
from jax import lax
from jax.sharding import PartitionSpec as P


def passed_along(x, axis, by):
    length = lax.axis_size(axis)
    return lax.ppermute(x, axis, [(i, (i + by) % length) for i in range(length)])


def slice_backward(pair_inputs, pair_scaled, gate_slice, up_slice, down_slice):
    contract_rows = (((0,), (0,)), ((), ()))
    contract_last = (((1,), (1,)), ((), ()))
    gate_pre = jnp.dot(pair_inputs, gate_slice, preferred_element_type=jnp.float32)
    up_pre = jnp.dot(pair_inputs, up_slice, preferred_element_type=jnp.float32)
    logistic = jax.nn.sigmoid(gate_pre)
    activated = gate_pre * logistic
    hidden = (activated * up_pre).astype(jnp.bfloat16)
    hidden_grad = lax.dot_general(
        pair_scaled, down_slice, contract_last, preferred_element_type=jnp.float32
    )
    gate_grad = (hidden_grad * up_pre * logistic * (1.0 + gate_pre * (1.0 - logistic))).astype(
        jnp.bfloat16
    )
    up_grad = (hidden_grad * activated).astype(jnp.bfloat16)
    down_total = lax.dot_general(
        hidden, pair_scaled, contract_rows, preferred_element_type=jnp.float32
    )
    gate_total = lax.dot_general(
        pair_inputs, gate_grad, contract_rows, preferred_element_type=jnp.float32
    )
    up_total = lax.dot_general(
        pair_inputs, up_grad, contract_rows, preferred_element_type=jnp.float32
    )
    partial_back = lax.dot_general(
        gate_grad, gate_slice, contract_last, preferred_element_type=jnp.float32
    )
    partial_back = partial_back + lax.dot_general(
        up_grad, up_slice, contract_last, preferred_element_type=jnp.float32
    )
    return (partial_back, gate_total, up_total, down_total)


def exchange(blocks, axis, sign):
    pieces = [blocks[0]]
    for shift in range(1, blocks.shape[0]):
        pieces.append(passed_along(blocks[shift], axis, sign * shift))
    return jnp.stack(pieces)


def along_x(x, sign):
    sections = lax.axis_size("section")
    halves = lax.axis_size("dpx")
    pairs = []
    for section in range(sections):
        low = section // 2
        for half in range(halves):
            if (low == 0) == (sign > 0):
                target = (section + 2 if low == 0 else section - 2, half)
            else:
                target = (section - 2 if low == 1 else section + 2, (half + sign) % halves)
            pairs.append((section * halves + half, target[0] * halves + target[1]))
    return lax.ppermute(x, ("section", "dpx"), pairs)


def to_x_partner(x):
    cut = x.shape[0] // 2
    ahead = along_x(along_x(x[:cut], 1), 1)
    behind = along_x(along_x(x[cut:], -1), -1)
    return jnp.concatenate([ahead, behind], axis=0)


def per_device(incoming, stash, expert_ids, route_weight, w_gate, w_up, w_down):
    arrived = passed_along(incoming, "section", -1)
    upstream = arrived[0]
    tokens = stash[0]
    mbatch, tok_rows, model_width = tokens.shape
    top_count = expert_ids.shape[-1]
    experts = lax.axis_size("expert")
    capacity = max(2, 3 * tok_rows * top_count // (2 * experts))
    pair_count = tok_rows * top_count
    slot_count = experts * capacity
    block_rows = mbatch * capacity
    lanes = 128
    flat_rows = block_rows * model_width // lanes
    chosen = expert_ids[0].reshape(mbatch, pair_count)
    onehot = (chosen[:, :, None] == jnp.arange(experts, dtype=jnp.int32)[None, None, :]).astype(
        jnp.int32
    )
    running = jnp.cumsum(onehot, axis=1) - 1
    position = jnp.sum(onehot * running, axis=2)
    relative = (chosen - lax.axis_index("expert")) % experts
    slot_index = relative * capacity + position
    pair_slot = slot_index[:, :, None] == jnp.arange(slot_count, dtype=jnp.int32)[None, None, :]
    token_slot = pair_slot.reshape(mbatch, tok_rows, top_count, slot_count).any(axis=2)
    token_slot = token_slot.astype(jnp.bfloat16)
    weight_pairs = route_weight[0].reshape(mbatch, pair_count)
    slot_weight = jnp.sum(jnp.where(pair_slot, weight_pairs[:, :, None], 0.0), axis=1)

    def to_slots(rows):
        return jnp.einsum("mts,mtd->msd", token_slot, rows, preferred_element_type=jnp.float32)

    def by_expert(slots):
        return (
            slots.reshape(mbatch, experts, capacity, model_width)
            .transpose(1, 0, 2, 3)
            .reshape(experts, flat_rows, lanes)
        )

    def dispatch(slots):
        arrived_blocks = exchange(slots, "expert", 1)
        rows = arrived_blocks.reshape(experts * block_rows, model_width)
        rows = jnp.concatenate([rows, to_x_partner(rows)], axis=0)
        return lax.all_gather(rows, "dpy", axis=0, tiled=True)

    input_rows = dispatch(by_expert(to_slots(tokens).astype(jnp.bfloat16)))
    scaled_rows = dispatch(
        by_expert((slot_weight[:, :, None] * to_slots(upstream)).astype(jnp.bfloat16))
    )
    gate_slice = w_gate[0, 0]
    up_slice = w_up[0, 0]
    down_slice = w_down[0, 0]
    partial_rows, gate_total, up_total, down_total = slice_backward(
        input_rows, scaled_rows, gate_slice, up_slice, down_slice
    )
    sent_back = partial_rows.astype(jnp.bfloat16)
    summed = lax.psum_scatter(sent_back, "dpy", scatter_dimension=0, tiled=True)
    summed, gate_total, up_total, down_total = lax.optimization_barrier(
        (summed, gate_total, up_total, down_total)
    )
    own_rows = summed.shape[0] // 2
    summed = (
        summed[:own_rows].astype(jnp.float32)
        + to_x_partner(summed[own_rows:]).astype(jnp.float32)
    ).astype(jnp.bfloat16)
    returned = exchange(summed.reshape(experts, flat_rows, lanes), "expert", -1)
    back_slots = (
        returned.reshape(experts, mbatch, capacity, model_width)
        .transpose(1, 0, 2, 3)
        .reshape(mbatch, slot_count, model_width)
    )
    pair_sum = jnp.einsum(
        "mts,msd->mtd", token_slot, back_slots, preferred_element_type=jnp.float32
    )
    input_grad = (upstream.astype(jnp.float32) + pair_sum).astype(jnp.bfloat16)
    grad_gate = gate_total.astype(jnp.bfloat16)[None, None]
    grad_up = up_total.astype(jnp.bfloat16)[None, None]
    grad_down = down_total.astype(jnp.bfloat16)[None, None]
    return (input_grad[None], grad_gate, grad_up, grad_down)


def solution(mesh):
    sections, replicas, experts = mesh.devices.shape
    split = jax.sharding.Mesh(
        mesh.devices.reshape(sections, replicas // 2, 2, experts),
        ("section", "dpy", "dpx", "expert"),
    )
    tokens = P("section", None, ("dpy", "dpx", "expert"), None)
    by_cols = P("section", "expert", None, ("dpy", "dpx"))
    by_rows = P("section", "expert", ("dpy", "dpx"), None)
    return jax.shard_map(
        per_device,
        mesh=split,
        in_specs=(tokens, tokens, tokens, tokens, by_cols, by_cols, by_rows),
        out_specs=(tokens, by_cols, by_cols, by_rows),
        check_vma=False,
    )
```

```python
import jax
import jax.numpy as jnp
from jax import lax
from jax.sharding import PartitionSpec as P


def passed_along(x, axis, by):
    length = lax.axis_size(axis)
    return lax.ppermute(x, axis, [(i, (i + by) % length) for i in range(length)])


def slice_backward(pair_inputs, pair_scaled, gate_slice, up_slice, down_slice):
    contract_rows = (((0,), (0,)), ((), ()))
    contract_last = (((1,), (1,)), ((), ()))
    gate_pre = jnp.dot(pair_inputs, gate_slice, preferred_element_type=jnp.float32)
    up_pre = jnp.dot(pair_inputs, up_slice, preferred_element_type=jnp.float32)
    logistic = jax.nn.sigmoid(gate_pre)
    activated = gate_pre * logistic
    hidden = (activated * up_pre).astype(jnp.bfloat16)
    hidden_grad = lax.dot_general(
        pair_scaled, down_slice, contract_last, preferred_element_type=jnp.float32
    )
    gate_grad = (hidden_grad * up_pre * logistic * (1.0 + gate_pre * (1.0 - logistic))).astype(
        jnp.bfloat16
    )
    up_grad = (hidden_grad * activated).astype(jnp.bfloat16)
    down_total = lax.dot_general(
        hidden, pair_scaled, contract_rows, preferred_element_type=jnp.float32
    )
    gate_total = lax.dot_general(
        pair_inputs, gate_grad, contract_rows, preferred_element_type=jnp.float32
    )
    up_total = lax.dot_general(
        pair_inputs, up_grad, contract_rows, preferred_element_type=jnp.float32
    )
    partial_back = lax.dot_general(
        jnp.concatenate([gate_grad, up_grad], axis=1),
        jnp.concatenate([gate_slice, up_slice], axis=1),
        contract_last,
        preferred_element_type=jnp.float32,
    )
    return (partial_back, gate_total, up_total, down_total)


def exchange(blocks, axis, sign):
    pieces = [blocks[0]]
    for shift in range(1, blocks.shape[0]):
        pieces.append(passed_along(blocks[shift], axis, sign * shift))
    return jnp.stack(pieces)


def along_x(x, sign):
    sections = lax.axis_size("section")
    halves = lax.axis_size("dpx")
    pairs = []
    for section in range(sections):
        low = section // 2
        for half in range(halves):
            if (low == 0) == (sign > 0):
                target = (section + 2 if low == 0 else section - 2, half)
            else:
                target = (section - 2 if low == 1 else section + 2, (half + sign) % halves)
            pairs.append((section * halves + half, target[0] * halves + target[1]))
    return lax.ppermute(x, ("section", "dpx"), pairs)


def to_x_partner(x):
    cut = x.shape[0] // 2
    ahead = along_x(along_x(x[:cut], 1), 1)
    behind = along_x(along_x(x[cut:], -1), -1)
    return jnp.concatenate([ahead, behind], axis=0)


def per_device(incoming, stash, expert_ids, route_weight, w_gate, w_up, w_down):
    arrived = passed_along(incoming, "section", -1)
    upstream = arrived[0]
    tokens = stash[0]
    mbatch, tok_rows, model_width = tokens.shape
    top_count = expert_ids.shape[-1]
    experts = lax.axis_size("expert")
    capacity = max(2, 3 * tok_rows * top_count // (2 * experts))
    pair_count = tok_rows * top_count
    slot_count = experts * capacity
    block_rows = mbatch * capacity
    lanes = 128
    flat_rows = block_rows * model_width // lanes
    chosen = expert_ids[0].reshape(mbatch, pair_count)
    onehot = (chosen[:, :, None] == jnp.arange(experts, dtype=jnp.int32)[None, None, :]).astype(
        jnp.int32
    )
    running = jnp.cumsum(onehot, axis=1) - 1
    position = jnp.sum(onehot * running, axis=2)
    relative = (chosen - lax.axis_index("expert")) % experts
    slot_index = relative * capacity + position
    pair_slot = slot_index[:, :, None] == jnp.arange(slot_count, dtype=jnp.int32)[None, None, :]
    token_slot = pair_slot.reshape(mbatch, tok_rows, top_count, slot_count).any(axis=2)
    token_slot = token_slot.astype(jnp.bfloat16)
    weight_pairs = route_weight[0].reshape(mbatch, pair_count)
    slot_weight = jnp.sum(jnp.where(pair_slot, weight_pairs[:, :, None], 0.0), axis=1)

    def to_slots(rows):
        return jnp.einsum("mts,mtd->msd", token_slot, rows, preferred_element_type=jnp.float32)

    def by_expert(slots):
        return (
            slots.reshape(mbatch, experts, capacity, model_width)
            .transpose(1, 0, 2, 3)
            .reshape(experts, flat_rows, lanes)
        )

    def dispatch(slots):
        arrived_blocks = exchange(slots, "expert", 1)
        rows = arrived_blocks.reshape(experts * block_rows, model_width)
        rows = jnp.concatenate([rows, to_x_partner(rows)], axis=0)
        return lax.all_gather(rows, "dpy", axis=0, tiled=True)

    input_rows = dispatch(by_expert(to_slots(tokens).astype(jnp.bfloat16)))
    scaled_rows = dispatch(
        by_expert((slot_weight[:, :, None] * to_slots(upstream)).astype(jnp.bfloat16))
    )
    gate_slice = w_gate[0, 0]
    up_slice = w_up[0, 0]
    down_slice = w_down[0, 0]
    partial_rows, gate_total, up_total, down_total = slice_backward(
        input_rows, scaled_rows, gate_slice, up_slice, down_slice
    )
    sent_back = partial_rows.astype(jnp.bfloat16)
    summed = lax.psum_scatter(sent_back, "dpy", scatter_dimension=0, tiled=True)
    own_rows = summed.shape[0] // 2
    summed = (
        summed[:own_rows].astype(jnp.float32)
        + to_x_partner(summed[own_rows:]).astype(jnp.float32)
    ).astype(jnp.bfloat16)
    returned = exchange(summed.reshape(experts, flat_rows, lanes), "expert", -1)
    back_slots = (
        returned.reshape(experts, mbatch, capacity, model_width)
        .transpose(1, 0, 2, 3)
        .reshape(mbatch, slot_count, model_width)
    )
    pair_sum = jnp.einsum(
        "mts,msd->mtd", token_slot, back_slots, preferred_element_type=jnp.float32
    )
    input_grad = (upstream.astype(jnp.float32) + pair_sum).astype(jnp.bfloat16)
    grad_gate = gate_total.astype(jnp.bfloat16)[None, None]
    grad_up = up_total.astype(jnp.bfloat16)[None, None]
    grad_down = down_total.astype(jnp.bfloat16)[None, None]
    return (input_grad[None], grad_gate, grad_up, grad_down)


def solution(mesh):
    sections, replicas, experts = mesh.devices.shape
    split = jax.sharding.Mesh(
        mesh.devices.reshape(sections, replicas // 2, 2, experts),
        ("section", "dpy", "dpx", "expert"),
    )
    tokens = P("section", None, ("dpy", "dpx", "expert"), None)
    by_cols = P("section", "expert", None, ("dpy", "dpx"))
    by_rows = P("section", "expert", ("dpy", "dpx"), None)
    return jax.shard_map(
        per_device,
        mesh=split,
        in_specs=(tokens, tokens, tokens, tokens, by_cols, by_cols, by_rows),
        out_specs=(tokens, by_cols, by_cols, by_rows),
        check_vma=False,
    )
```

```python
import jax
import jax.numpy as jnp
from jax import lax
from jax.sharding import PartitionSpec as P


def passed_along(x, axis, by):
    length = lax.axis_size(axis)
    return lax.ppermute(x, axis, [(i, (i + by) % length) for i in range(length)])


def slice_backward(pair_inputs, pair_scaled, gate_slice, up_slice, down_slice):
    contract_rows = (((0,), (0,)), ((), ()))
    contract_last = (((1,), (1,)), ((), ()))
    gate_pre = jnp.dot(pair_inputs, gate_slice, preferred_element_type=jnp.float32)
    up_pre = jnp.dot(pair_inputs, up_slice, preferred_element_type=jnp.float32)
    logistic = jax.nn.sigmoid(gate_pre)
    activated = gate_pre * logistic
    hidden = (activated * up_pre).astype(jnp.bfloat16)
    hidden_grad = lax.dot_general(
        pair_scaled, down_slice, contract_last, preferred_element_type=jnp.float32
    )
    gate_grad = (hidden_grad * up_pre * logistic * (1.0 + gate_pre * (1.0 - logistic))).astype(
        jnp.bfloat16
    )
    up_grad = (hidden_grad * activated).astype(jnp.bfloat16)
    down_total = lax.dot_general(
        hidden, pair_scaled, contract_rows, preferred_element_type=jnp.float32
    )
    gate_total = lax.dot_general(
        pair_inputs, gate_grad, contract_rows, preferred_element_type=jnp.float32
    )
    up_total = lax.dot_general(
        pair_inputs, up_grad, contract_rows, preferred_element_type=jnp.float32
    )
    partial_back = lax.dot_general(
        gate_grad, gate_slice, contract_last, preferred_element_type=jnp.float32
    )
    partial_back = partial_back + lax.dot_general(
        up_grad, up_slice, contract_last, preferred_element_type=jnp.float32
    )
    return (partial_back, gate_total, up_total, down_total)


def exchange(blocks, axis, sign):
    pieces = [blocks[0]]
    for shift in range(1, blocks.shape[0]):
        pieces.append(passed_along(blocks[shift], axis, sign * shift))
    return jnp.stack(pieces)


def along_x(x, sign):
    sections = lax.axis_size("section")
    halves = lax.axis_size("dpx")
    pairs = []
    for section in range(sections):
        low = section // 2
        for half in range(halves):
            if (low == 0) == (sign > 0):
                target = (section + 2 if low == 0 else section - 2, half)
            else:
                target = (section - 2 if low == 1 else section + 2, (half + sign) % halves)
            pairs.append((section * halves + half, target[0] * halves + target[1]))
    return lax.ppermute(x, ("section", "dpx"), pairs)


def to_x_partner(x):
    cut = x.shape[0] // 2
    ahead = along_x(along_x(x[:cut], 1), 1)
    behind = along_x(along_x(x[cut:], -1), -1)
    return jnp.concatenate([ahead, behind], axis=0)


def per_device(incoming, stash, expert_ids, route_weight, w_gate, w_up, w_down):
    arrived = passed_along(incoming, "section", -1)
    upstream = arrived[0]
    tokens = stash[0]
    mbatch, tok_rows, model_width = tokens.shape
    top_count = expert_ids.shape[-1]
    experts = lax.axis_size("expert")
    capacity = max(2, 3 * tok_rows * top_count // (2 * experts))
    pair_count = tok_rows * top_count
    slot_count = experts * capacity
    block_rows = mbatch * capacity
    lanes = 128
    flat_rows = block_rows * model_width // lanes
    chosen = expert_ids[0].reshape(mbatch, pair_count)
    onehot = (chosen[:, :, None] == jnp.arange(experts, dtype=jnp.int32)[None, None, :]).astype(
        jnp.int32
    )
    running = jnp.cumsum(onehot, axis=1) - 1
    position = jnp.sum(onehot * running, axis=2)
    relative = (chosen - lax.axis_index("expert")) % experts
    slot_index = relative * capacity + position
    pair_slot = slot_index[:, :, None] == jnp.arange(slot_count, dtype=jnp.int32)[None, None, :]
    token_slot = pair_slot.reshape(mbatch, tok_rows, top_count, slot_count).any(axis=2)
    token_slot = token_slot.astype(jnp.bfloat16)
    weight_pairs = route_weight[0].reshape(mbatch, pair_count)
    slot_weight = jnp.sum(jnp.where(pair_slot, weight_pairs[:, :, None], 0.0), axis=1)

    def to_slots(rows):
        return jnp.einsum("mts,mtd->msd", token_slot, rows, preferred_element_type=jnp.float32)

    def by_expert(slots):
        return (
            slots.reshape(mbatch, experts, capacity, model_width)
            .transpose(1, 0, 2, 3)
            .reshape(experts, flat_rows, lanes)
        )

    here = lax.axis_index("expert")

    def dispatch(slots, joint):
        if joint:
            received = lax.all_to_all(jnp.roll(slots, here, axis=0), "expert", 0, 0, tiled=True)
            flipped = jnp.concatenate([received[:1], received[1:][::-1]], axis=0)
            arrived_blocks = jnp.roll(flipped, here, axis=0)
        else:
            arrived_blocks = exchange(slots, "expert", 1)
        rows = arrived_blocks.reshape(experts * block_rows, model_width)
        rows = jnp.concatenate([rows, to_x_partner(rows)], axis=0)
        return lax.all_gather(rows, "dpy", axis=0, tiled=True)

    input_rows = dispatch(by_expert(to_slots(tokens).astype(jnp.bfloat16)), True)
    scaled_rows = dispatch(
        by_expert((slot_weight[:, :, None] * to_slots(upstream)).astype(jnp.bfloat16)), False
    )
    gate_slice = w_gate[0, 0]
    up_slice = w_up[0, 0]
    down_slice = w_down[0, 0]
    partial_rows, gate_total, up_total, down_total = slice_backward(
        input_rows, scaled_rows, gate_slice, up_slice, down_slice
    )
    sent_back = partial_rows.astype(jnp.bfloat16)
    summed = lax.psum_scatter(sent_back, "dpy", scatter_dimension=0, tiled=True)
    own_rows = summed.shape[0] // 2
    summed = (
        summed[:own_rows].astype(jnp.float32)
        + to_x_partner(summed[own_rows:]).astype(jnp.float32)
    ).astype(jnp.bfloat16)
    returned = exchange(summed.reshape(experts, flat_rows, lanes), "expert", -1)
    back_slots = (
        returned.reshape(experts, mbatch, capacity, model_width)
        .transpose(1, 0, 2, 3)
        .reshape(mbatch, slot_count, model_width)
    )
    pair_sum = jnp.einsum(
        "mts,msd->mtd", token_slot, back_slots, preferred_element_type=jnp.float32
    )
    input_grad = (upstream.astype(jnp.float32) + pair_sum).astype(jnp.bfloat16)
    grad_gate = gate_total.astype(jnp.bfloat16)[None, None]
    grad_up = up_total.astype(jnp.bfloat16)[None, None]
    grad_down = down_total.astype(jnp.bfloat16)[None, None]
    return (input_grad[None], grad_gate, grad_up, grad_down)


def solution(mesh):
    sections, replicas, experts = mesh.devices.shape
    split = jax.sharding.Mesh(
        mesh.devices.reshape(sections, replicas // 2, 2, experts),
        ("section", "dpy", "dpx", "expert"),
    )
    tokens = P("section", None, ("dpy", "dpx", "expert"), None)
    by_cols = P("section", "expert", None, ("dpy", "dpx"))
    by_rows = P("section", "expert", ("dpy", "dpx"), None)
    return jax.shard_map(
        per_device,
        mesh=split,
        in_specs=(tokens, tokens, tokens, tokens, by_cols, by_cols, by_rows),
        out_specs=(tokens, by_cols, by_cols, by_rows),
        check_vma=False,
    )
```
